128 devices in a mesh: expert: 128 (over y, z, x, core).
Axes of the slice: x: 4, y: 4, z: 4, core: 2. Of those that a mesh axis runs over, the one named last changes fastest.
Arguments:
- tokens: bfloat16 [8192, 3584], P('expert'), may hold values from -6 to 6
- expert_ids: int32 [8192, 8], P('expert'), may hold values from 0 to 127, all different within a row; in each aligned block of 64 rows (0 to 63, 64 to 127, ...) at most 6 rows name the same one
- gate_weights: float32 [8192, 8], P('expert'), may hold values from 0.05 to 1
- host: int32 [128], replicated, may hold values from 0 to 127, each once
- w_in: bfloat16 [128, 2, 3584, 2, 512], P('expert'), may hold values from -0.09375 to 0.09375
- w_out: bfloat16 [128, 2, 512, 3584], P('expert'), may hold values from -0.1875 to 0.1875
Outputs:
- moe_out: bfloat16 [8192, 3584], P('expert')
The draws below stay inside these ranges and needn't reach their ends.
Inputs may be any that keep to these rules, and one draw needn't show every extreme that they name: `expert_ids`: each row names 8 different experts; in the rows of one device no expert is named more than 6 times, a bound that some block reaches. A permutation: device d holds the weights of expert host[d].
All inputs are finite; a program needn't handle non-finite values.
Results may differ from the reference program's by a relative error of at most 0.011.
Values may be sent and summed in bfloat16 or wider, within the bound.
No kernel may reach another device: no remote copies, remote signals or barrier semaphores. Data moves between devices by JAX's collectives and lax.ppermute only.
A program may use at most 192 MiB of HBM per device.

```python
import math
import jax
import jax.numpy as jnp
import numpy as np
from jax import lax

D = 3584
FFW = 1024
TOP = 8
TOK_DEV = 64
HALF = 512
EXPERTS = 128
MOST = 6
TOKENS = 8192
N_EXPERT = 128


def level_of(rng, dims, shards, low, largest):
    def one(dim, parts):
        steps = jax.random.uniform(jax.random.fold_in(jax.random.fold_in(rng, 6), dim), (parts,), jnp.float32, low / len(shards), largest / len(shards))
        return jnp.repeat(jnp.exp(steps), dims[dim] // parts).reshape((-1,) + (1,) * (len(dims) - dim - 1))

    loudness = one(*shards[0])
    for cut in shards[1:]:
        loudness = loudness * one(*cut)
    return loudness


def deal_out(own_key, own, number, rows, number_of, top, limit, slope):
    ranking = jax.random.permutation(own_key, number_of)
    packed, common = portions_of(number_of, rows * top, limit, slope, True), portions_of(number_of, rows * top, limit, slope, False)
    places = jnp.arange(number_of)

    def named(sizes, turn):
        used = int((sizes > 0).sum())
        fixed = max(1, used // 4)
        moved = fixed + (places - fixed + turn * (used - fixed)) % max(1, number_of - fixed)
        return jnp.zeros((number_of,), jnp.int32).at[ranking[jnp.where(places < fixed, places, moved)]].set(jnp.asarray(sizes, jnp.int32))

    sizes = jnp.where(number % 4 == 0, named(packed, number // 4), named(common, number - number // 4 - 1))
    mixed = jax.random.permutation(jax.random.fold_in(own, 3), number_of)
    giver, sink = mixed[0:number_of // 2 * 2:2], mixed[1:number_of // 2 * 2:2]
    room = jnp.minimum(sizes[giver] - 1, limit - sizes[sink]) // 2
    room = jnp.where((giver == ranking[0]) | (sink == ranking[0]) | (sizes[sink] == 0), 0, jnp.maximum(room, 0))
    moved = jax.random.randint(jax.random.fold_in(own, 4), (number_of // 2,), 0, 1 << 20) % (room + 1)
    sizes = sizes.at[giver].add(-moved).at[sink].add(moved)
    items = jnp.searchsorted(jnp.cumsum(sizes), jnp.arange(rows * top), side="right").astype(jnp.int32)
    grid = items.reshape(top, rows).T
    grid = grid[jax.random.permutation(jax.random.fold_in(own, 1), rows)]
    turn = jax.random.randint(jax.random.fold_in(own, 2), (rows, 1), 0, top)
    return jnp.take_along_axis(grid, (jnp.arange(top)[None, :] + turn) % top, axis=1)


def portions_of(count, total, reach, lean, full):
    portions = [(1 << 20) // math.isqrt(grade ** lean) + 1 for grade in range(1, count + 1)]
    largest = reach if full else min(reach, max(-(-total // count), total * portions[0] // sum(portions)))
    least = 1 if total - largest >= count - 1 else 0
    counts, surplus = [largest] + [least] * (count - 1), total - largest - least * (count - 1)
    while surplus > 0:
        candidates = [i for i in range(1, count) if counts[i] < largest] or [i for i in range(1, count) if counts[i] < reach]
        mass, left = sum([portions[i] for i in candidates]), surplus
        for i in candidates:
            addition = min(reach - counts[i], max(1, left * portions[i] // mass), surplus)
            counts[i] = counts[i] + addition
            surplus = surplus - addition
    return np.array(counts)


def normal_values(stream_key, dims, spread, reach, cuts=(), kind=jnp.bfloat16):
    array = jax.random.normal(stream_key, dims, jnp.float32) * spread
    if len(cuts) > 0:
        array = level_of(stream_key, dims, cuts, -0.22, 0.18) * array
    return jnp.clip(array, min=-reach, max=reach).astype(kind)


def setup_inputs(seed: int = 0) -> dict:
    streams_of = jax.random.split(jax.random.key(seed), 7)
    tokens = normal_values(streams_of[0], (TOKENS, D), 1.0, 6.0, ((0, 128),))
    expert_ids_keys = jax.random.split(jax.random.fold_in(streams_of[1], 1), TOKENS // TOK_DEV)
    expert_ids_turns = jax.random.permutation(jax.random.fold_in(streams_of[1], 3), TOKENS // TOK_DEV)
    expert_ids = jax.vmap(lambda own, number: deal_out(jax.random.fold_in(streams_of[1], 2), own, number, TOK_DEV, EXPERTS, TOP, MOST, 2))(expert_ids_keys, expert_ids_turns).reshape((TOKENS, TOP))
    gate_weights = jnp.clip(jnp.exp(math.log(1.0) - 2.9957323 * jax.random.uniform(streams_of[2], (TOKENS, TOP), jnp.float32) ** level_of(streams_of[2], (TOKENS, TOP), ((0, 128),), -0.2, 0.2)), 0.05, 1.0)
    host = jax.random.permutation(streams_of[3], EXPERTS).astype(jnp.int32)
    w_in = normal_values(streams_of[4], (EXPERTS, 2, D, 2, HALF), D ** -0.5, 0.09375, ((0, 128),))
    w_out = normal_values(streams_of[5], (EXPERTS, 2, HALF, D), FFW ** -0.5, 0.1875, ((0, 128),))
    return {"tokens": tokens, "expert_ids": expert_ids, "gate_weights": gate_weights, "host": host, "w_in": w_in, "w_out": w_out}


def reference(tokens, expert_ids, gate_weights, host, w_in, w_out):
    capacity = N_EXPERT * MOST
    flat_experts = expert_ids.reshape(-1).astype(jnp.int32)
    flat_gates = gate_weights.reshape(-1)
    total = flat_experts.shape[0]
    assignment = jnp.arange(total, dtype=jnp.int32)
    source = assignment // (TOK_DEV * TOP)
    onehot = (flat_experts[:, None] == jnp.arange(EXPERTS, dtype=jnp.int32)[None, :]).astype(jnp.int32)
    running = jnp.cumsum(onehot.reshape(N_EXPERT, TOK_DEV * TOP, EXPERTS), axis=1).reshape(total, EXPERTS)
    within = jnp.sum(running * onehot, axis=1) - 1
    slot = source * MOST + within
    table = jnp.full((EXPERTS, capacity), total, jnp.int32).at[flat_experts, slot].set(assignment)

    def one_expert(result, items):
        expert, first, second = items
        chosen = table[expert]
        valid = chosen < total
        safe = jnp.minimum(chosen, total - 1)
        token_rows = safe // TOP
        inputs = tokens[token_rows].astype(jnp.float32)
        projected = jnp.einsum("rd,hdgu->rhgu", inputs, first.astype(jnp.float32))
        hidden = (jax.nn.silu(projected[:, :, 0]) * projected[:, :, 1]).astype(jnp.bfloat16)
        output = jnp.einsum("rhu,hud->rd", hidden.astype(jnp.float32), second.astype(jnp.float32))
        output = output.astype(jnp.bfloat16).astype(jnp.float32)
        weight = jnp.where(valid, flat_gates[safe], jnp.float32(0.0))
        return result.at[token_rows].add(weight[:, None] * output), None

    start = jnp.zeros((tokens.shape[0], tokens.shape[1]), jnp.float32)
    result, _ = lax.scan(one_expert, start, (host.astype(jnp.int32), w_in, w_out))
    return result.astype(jnp.bfloat16)
```

```python
import jax
import jax.numpy as jnp
from jax import lax
from jax.sharding import PartitionSpec as P

MOST = 6


def expert_ffn(rows, first_weights, second_weights):
    projected = jnp.einsum(
        "esd,hdgu->eshgu", rows, first_weights, preferred_element_type=jnp.float32
    )
    hidden = (jax.nn.silu(projected[:, :, :, 0]) * projected[:, :, :, 1]).astype(jnp.bfloat16)
    output = jnp.einsum(
        "eshu,hud->esd", hidden, second_weights, preferred_element_type=jnp.float32
    )
    return output.astype(jnp.bfloat16)


def local(tokens, expert_ids, gate_weights, host, w_in, w_out):
    experts = lax.axis_size("expert")
    tok_dev, top_count = expert_ids.shape
    d_model = tokens.shape[1]
    slot_count = MOST
    capacity = experts * slot_count
    expert_range = jnp.arange(experts, dtype=jnp.int32)
    placed = (host[:, None] == expert_range[None, :]).astype(jnp.int32)
    holder = jnp.sum(placed * expert_range[:, None], axis=0)
    flat_experts = expert_ids.reshape(-1)
    onehot = (flat_experts[:, None] == expert_range[None, :]).astype(jnp.int32)
    within = jnp.sum(jnp.cumsum(onehot, axis=0) * onehot, axis=1) - 1
    target = jnp.sum(onehot * holder[None, :], axis=1)
    position = (target * slot_count + within).reshape(tok_dev, top_count)
    slots = jnp.arange(capacity, dtype=jnp.int32)
    hit = position[None, :, :] == slots[:, None, None]
    dispatch = jnp.any(hit, axis=2).astype(jnp.bfloat16).reshape(experts, slot_count, tok_dev)
    outgoing = jnp.einsum(
        "esk,kd->esd", dispatch, tokens, preferred_element_type=jnp.float32
    ).astype(jnp.bfloat16)
    received = lax.all_to_all(
        outgoing,
        "expert",
        split_axis=0,
        concat_axis=0,
        tiled=True,
    )
    expert_out = expert_ffn(received, w_in[0], w_out[0])
    answered = lax.all_to_all(
        expert_out,
        "expert",
        split_axis=0,
        concat_axis=0,
        tiled=True,
    )
    combine = jnp.sum(
        jnp.where(hit, gate_weights[None, :, :], jnp.float32(0.0)), axis=2
    ).T.reshape(tok_dev, experts, slot_count)
    combine_hi = combine.astype(jnp.bfloat16)
    combine_lo = (combine - combine_hi.astype(jnp.float32)).astype(jnp.bfloat16)
    weighted = jnp.einsum(
        "tes,esd->td", combine_hi, answered, preferred_element_type=jnp.float32
    ) + jnp.einsum("tes,esd->td", combine_lo, answered, preferred_element_type=jnp.float32)
    return weighted.astype(jnp.bfloat16)


def solution(mesh):
    in_specs = (
        P("expert", None),
        P("expert", None),
        P("expert", None),
        P(),
        P("expert", None, None, None, None),
        P("expert", None, None, None),
    )
    out_specs = P("expert", None)
    return jax.shard_map(local, mesh=mesh, in_specs=in_specs, out_specs=out_specs, check_vma=False)
```

```python
import jax
import jax.numpy as jnp
from jax import lax
from jax.sharding import PartitionSpec as P

MOST = 6


def expert_ffn(rows, first_weights, second_weights):
    projected = jnp.einsum(
        "rd,hdgu->rhgu", rows, first_weights, preferred_element_type=jnp.float32
    )
    hidden = (jax.nn.silu(projected[:, :, 0]) * projected[:, :, 1]).astype(jnp.bfloat16)
    output = jnp.einsum(
        "rhu,hud->rd", hidden, second_weights, preferred_element_type=jnp.float32
    )
    return output.astype(jnp.bfloat16)


def local(tokens, expert_ids, gate_weights, host, w_in, w_out):
    experts = lax.axis_size("expert")
    tok_dev, top_count = expert_ids.shape
    d_model = tokens.shape[1]
    slot_count = MOST
    capacity = experts * slot_count
    expert_range = jnp.arange(experts, dtype=jnp.int32)
    placed = (host[:, None] == expert_range[None, :]).astype(jnp.int32)
    holder = jnp.sum(placed * expert_range[:, None], axis=0)
    flat_experts = expert_ids.reshape(-1)
    onehot = (flat_experts[:, None] == expert_range[None, :]).astype(jnp.int32)
    within = jnp.sum(jnp.cumsum(onehot, axis=0) * onehot, axis=1) - 1
    target = jnp.sum(onehot * holder[None, :], axis=1)
    position = (target * slot_count + within).reshape(tok_dev, top_count)
    slots = jnp.arange(capacity, dtype=jnp.int32)
    hit = position[None, :, :] == slots[:, None, None]
    dispatch = jnp.any(hit, axis=2).astype(jnp.bfloat16)
    outgoing = jnp.dot(dispatch, tokens, preferred_element_type=jnp.float32).astype(jnp.bfloat16)
    lane_rows = slot_count * d_model // 128
    received = lax.all_to_all(
        outgoing.reshape(experts, lane_rows, 128),
        "expert",
        split_axis=0,
        concat_axis=0,
        tiled=True,
    )
    expert_out = expert_ffn(received.reshape(capacity, d_model), w_in[0], w_out[0])
    answered = lax.all_to_all(
        expert_out.reshape(experts, lane_rows, 128),
        "expert",
        split_axis=0,
        concat_axis=0,
        tiled=True,
    ).reshape(capacity, d_model)
    combine = jnp.sum(
        jnp.where(hit, gate_weights[None, :, :], jnp.float32(0.0)), axis=2
    ).T
    combine_hi = combine.astype(jnp.bfloat16)
    combine_lo = (combine - combine_hi.astype(jnp.float32)).astype(jnp.bfloat16)
    both = jnp.dot(
        jnp.concatenate([combine_hi, combine_lo], axis=0),
        answered,
        preferred_element_type=jnp.float32,
    )
    weighted = both[:tok_dev] + both[tok_dev:]
    return weighted.astype(jnp.bfloat16)


def solution(mesh):
    in_specs = (
        P("expert", None),
        P("expert", None),
        P("expert", None),
        P(),
        P("expert", None, None, None, None),
        P("expert", None, None, None),
    )
    out_specs = P("expert", None)
    return jax.shard_map(local, mesh=mesh, in_specs=in_specs, out_specs=out_specs, check_vma=False)
```

```python
import jax
import jax.numpy as jnp
from jax import lax
from jax.sharding import PartitionSpec as P

MOST = 6
CHUNK = 2


def expert_ffn(rows, first_weights, second_weights):
    projected = jnp.einsum(
        "rd,hdgu->rhgu", rows, first_weights, preferred_element_type=jnp.float32
    )
    hidden = (jax.nn.silu(projected[:, :, 0]) * projected[:, :, 1]).astype(jnp.bfloat16)
    output = jnp.einsum(
        "rhu,hud->rd", hidden, second_weights, preferred_element_type=jnp.float32
    )
    return output.astype(jnp.bfloat16)


def local(tokens, expert_ids, gate_weights, host, w_in, w_out):
    experts = lax.axis_size("expert")
    tok_dev, top_count = expert_ids.shape
    d_model = tokens.shape[1]
    slot_count = MOST
    capacity = experts * slot_count
    expert_range = jnp.arange(experts, dtype=jnp.int32)
    placed = (host[:, None] == expert_range[None, :]).astype(jnp.int32)
    holder = jnp.sum(placed * expert_range[:, None], axis=0)
    flat_experts = expert_ids.reshape(-1)
    onehot = (flat_experts[:, None] == expert_range[None, :]).astype(jnp.int32)
    within = jnp.sum(jnp.cumsum(onehot, axis=0) * onehot, axis=1) - 1
    target = jnp.sum(onehot * holder[None, :], axis=1)
    chunk_rows = experts * CHUNK
    lane_rows = CHUNK * d_model // 128
    chunk_of = (within // CHUNK).reshape(tok_dev, top_count)
    row_of = (target * CHUNK + within % CHUNK).reshape(tok_dev, top_count)
    rows = jnp.arange(chunk_rows, dtype=jnp.int32)
    both = None
    for chunk in range(slot_count // CHUNK):
        hit = (row_of[None, :, :] == rows[:, None, None]) & (chunk_of == chunk)[None, :, :]
        dispatch = jnp.any(hit, axis=2).astype(jnp.bfloat16)
        outgoing = jnp.dot(dispatch, tokens, preferred_element_type=jnp.float32).astype(jnp.bfloat16)
        received = lax.all_to_all(
            outgoing.reshape(experts, lane_rows, 128),
            "expert",
            split_axis=0,
            concat_axis=0,
            tiled=True,
        )
        expert_out = expert_ffn(received.reshape(chunk_rows, d_model), w_in[0], w_out[0])
        answered = lax.all_to_all(
            expert_out.reshape(experts, lane_rows, 128),
            "expert",
            split_axis=0,
            concat_axis=0,
            tiled=True,
        ).reshape(chunk_rows, d_model)
        combine = jnp.sum(
            jnp.where(hit, gate_weights[None, :, :], jnp.float32(0.0)), axis=2
        ).T
        combine_hi = combine.astype(jnp.bfloat16)
        combine_lo = (combine - combine_hi.astype(jnp.float32)).astype(jnp.bfloat16)
        part = jnp.dot(
            jnp.concatenate([combine_hi, combine_lo], axis=0),
            answered,
            preferred_element_type=jnp.float32,
        )
        both = part if both is None else both + part
    weighted = both[:tok_dev] + both[tok_dev:]
    return weighted.astype(jnp.bfloat16)


def solution(mesh):
    in_specs = (
        P("expert", None),
        P("expert", None),
        P("expert", None),
        P(),
        P("expert", None, None, None, None),
        P("expert", None, None, None),
    )
    out_specs = P("expert", None)
    return jax.shard_map(local, mesh=mesh, in_specs=in_specs, out_specs=out_specs, check_vma=False)
```

```python
import jax
import jax.numpy as jnp
from jax import lax
from jax.sharding import PartitionSpec as P

MOST = 6
CHUNK = 2
PIECES = 4


def expert_ffn(rows, first_weights, second_weights):
    projected = jnp.einsum(
        "rd,hdgu->rhgu", rows, first_weights, preferred_element_type=jnp.float32
    )
    hidden = (jax.nn.silu(projected[:, :, 0]) * projected[:, :, 1]).astype(jnp.bfloat16)
    output = jnp.einsum(
        "rhu,hud->rd", hidden, second_weights, preferred_element_type=jnp.float32
    )
    return output.astype(jnp.bfloat16)


def local(tokens, expert_ids, gate_weights, host, w_in, w_out):
    experts = lax.axis_size("expert")
    tok_dev, top_count = expert_ids.shape
    d_model = tokens.shape[1]
    slot_count = MOST
    capacity = experts * slot_count
    expert_range = jnp.arange(experts, dtype=jnp.int32)
    placed = (host[:, None] == expert_range[None, :]).astype(jnp.int32)
    holder = jnp.sum(placed * expert_range[:, None], axis=0)
    flat_experts = expert_ids.reshape(-1)
    onehot = (flat_experts[:, None] == expert_range[None, :]).astype(jnp.int32)
    within = jnp.sum(jnp.cumsum(onehot, axis=0) * onehot, axis=1) - 1
    target = jnp.sum(onehot * holder[None, :], axis=1)
    chunk_rows = experts * CHUNK
    piece = d_model // PIECES
    chunk_of = (within // CHUNK).reshape(tok_dev, top_count)
    row_of = (target * CHUNK + within % CHUNK).reshape(tok_dev, top_count)
    rows = jnp.arange(chunk_rows, dtype=jnp.int32)
    same_piece = jnp.eye(PIECES, dtype=jnp.bool_)
    token_pieces = tokens.reshape(tok_dev * PIECES, piece)
    both = None
    for chunk in range(slot_count // CHUNK):
        hit = (row_of[None, :, :] == rows[:, None, None]) & (chunk_of == chunk)[None, :, :]
        taken = jnp.any(hit, axis=2)
        dispatch = (taken[:, None, :, None] & same_piece[None, :, None, :]).astype(jnp.bfloat16)
        dispatch = dispatch.reshape(chunk_rows * PIECES, tok_dev * PIECES)
        outgoing = jnp.dot(dispatch, token_pieces, preferred_element_type=jnp.float32).astype(jnp.bfloat16)
        received = lax.all_to_all(
            outgoing.reshape(experts, CHUNK * PIECES, piece),
            "expert",
            split_axis=0,
            concat_axis=0,
            tiled=True,
        )
        expert_out = expert_ffn(received.reshape(chunk_rows, d_model), w_in[0], w_out[0])
        answered = lax.all_to_all(
            expert_out.reshape(experts, CHUNK * PIECES, piece),
            "expert",
            split_axis=0,
            concat_axis=0,
            tiled=True,
        ).reshape(chunk_rows * PIECES, piece)
        combine = jnp.sum(
            jnp.where(hit, gate_weights[None, :, :], jnp.float32(0.0)), axis=2
        ).T
        combine_hi = combine.astype(jnp.bfloat16)
        combine_lo = (combine - combine_hi.astype(jnp.float32)).astype(jnp.bfloat16)
        stacked = jnp.concatenate([combine_hi, combine_lo], axis=0)
        spread = jnp.where(
            same_piece[None, :, None, :], stacked[:, None, :, None], jnp.bfloat16(0)
        ).reshape(2 * tok_dev * PIECES, chunk_rows * PIECES)
        part = jnp.dot(spread, answered, preferred_element_type=jnp.float32)
        both = part if both is None else both + part
    half = tok_dev * PIECES
    weighted = (both[:half] + both[half:]).reshape(tok_dev, d_model)
    return weighted.astype(jnp.bfloat16)


def solution(mesh):
    in_specs = (
        P("expert", None),
        P("expert", None),
        P("expert", None),
        P(),
        P("expert", None, None, None, None),
        P("expert", None, None, None),
    )
    out_specs = P("expert", None)
    return jax.shard_map(local, mesh=mesh, in_specs=in_specs, out_specs=out_specs, check_vma=False)
```

```python
import jax
import jax.numpy as jnp
from jax import lax
from jax.sharding import PartitionSpec as P

MOST = 6
CHUNK = 2
PIECES = 4


def expert_ffn(rows, first_weights, second_weights):
    projected = jnp.einsum(
        "rd,hdgu->rhgu", rows, first_weights, preferred_element_type=jnp.float32
    )
    hidden = (jax.nn.silu(projected[:, :, 0]) * projected[:, :, 1]).astype(jnp.bfloat16)
    output = jnp.einsum(
        "rhu,hud->rd", hidden, second_weights, preferred_element_type=jnp.float32
    )
    return output.astype(jnp.bfloat16)


def local(tokens, expert_ids, gate_weights, host, w_in, w_out):
    experts = lax.axis_size("expert")
    tok_dev, top_count = expert_ids.shape
    d_model = tokens.shape[1]
    slot_count = MOST
    capacity = experts * slot_count
    expert_range = jnp.arange(experts, dtype=jnp.int32)
    placed = (host[:, None] == expert_range[None, :]).astype(jnp.int32)
    holder = jnp.sum(placed * expert_range[:, None], axis=0)
    flat_experts = expert_ids.reshape(-1)
    onehot = (flat_experts[:, None] == expert_range[None, :]).astype(jnp.int32)
    within = jnp.sum(jnp.cumsum(onehot, axis=0) * onehot, axis=1) - 1
    target = jnp.sum(onehot * holder[None, :], axis=1)
    chunk_rows = experts * CHUNK
    piece = d_model // PIECES
    chunk_of = (within // CHUNK).reshape(tok_dev, top_count)
    row_of = (target * CHUNK + within % CHUNK).reshape(tok_dev, top_count)
    token_pieces = tokens.reshape(tok_dev * PIECES, piece)
    piece_rows = jnp.arange(tok_dev * PIECES, dtype=jnp.int32)
    piece_cols = jnp.arange(chunk_rows * PIECES, dtype=jnp.int32)
    same_piece = (piece_rows[:, None] % PIECES) == (piece_cols[None, :] % PIECES)
    slot_col = piece_cols[None, :] // PIECES
    chunk_rep = jnp.repeat(chunk_of, PIECES, axis=0)
    row_rep = jnp.repeat(row_of, PIECES, axis=0)
    gate_rep = jnp.repeat(gate_weights, PIECES, axis=0)
    both = None
    for chunk in range(slot_count // CHUNK):
        slot_id = jnp.where(chunk_rep == chunk, row_rep, -1)
        taken = jnp.zeros((tok_dev * PIECES, chunk_rows * PIECES), jnp.bool_)
        combine = jnp.zeros((tok_dev * PIECES, chunk_rows * PIECES), jnp.float32)
        for k in range(top_count):
            match = slot_id[:, k : k + 1] == slot_col
            taken = taken | match
            combine = combine + jnp.where(match, gate_rep[:, k : k + 1], jnp.float32(0.0))
        taken = taken & same_piece
        combine = jnp.where(same_piece, combine, jnp.float32(0.0))
        dispatch = taken.T.astype(jnp.bfloat16)
        outgoing = jnp.dot(dispatch, token_pieces, preferred_element_type=jnp.float32).astype(jnp.bfloat16)
        received = lax.all_to_all(
            outgoing.reshape(experts, CHUNK * PIECES, piece),
            "expert",
            split_axis=0,
            concat_axis=0,
            tiled=True,
        )
        expert_out = expert_ffn(received.reshape(chunk_rows, d_model), w_in[0], w_out[0])
        answered = lax.all_to_all(
            expert_out.reshape(experts, CHUNK * PIECES, piece),
            "expert",
            split_axis=0,
            concat_axis=0,
            tiled=True,
        ).reshape(chunk_rows * PIECES, piece)
        combine_hi = combine.astype(jnp.bfloat16)
        combine_lo = (combine - combine_hi.astype(jnp.float32)).astype(jnp.bfloat16)
        stacked = jnp.concatenate([combine_hi, combine_lo], axis=0)
        part = jnp.dot(stacked, answered, preferred_element_type=jnp.float32)
        both = part if both is None else both + part
    half = tok_dev * PIECES
    weighted = (both[:half] + both[half:]).reshape(tok_dev, d_model)
    return weighted.astype(jnp.bfloat16)


def solution(mesh):
    in_specs = (
        P("expert", None),
        P("expert", None),
        P("expert", None),
        P(),
        P("expert", None, None, None, None),
        P("expert", None, None, None),
    )
    out_specs = P("expert", None)
    return jax.shard_map(local, mesh=mesh, in_specs=in_specs, out_specs=out_specs, check_vma=False)
```

```python
import jax
import jax.numpy as jnp
from jax import lax
from jax.sharding import PartitionSpec as P

MOST = 6
CHUNKS = (2, 4)
PIECES = 4


def expert_ffn(rows, first_weights, second_weights):
    projected = jnp.einsum(
        "rd,hdgu->rhgu", rows, first_weights, preferred_element_type=jnp.float32
    )
    hidden = (jax.nn.silu(projected[:, :, 0]) * projected[:, :, 1]).astype(jnp.bfloat16)
    output = jnp.einsum(
        "rhu,hud->rd", hidden, second_weights, preferred_element_type=jnp.float32
    )
    return output.astype(jnp.bfloat16)


def local(tokens, expert_ids, gate_weights, host, w_in, w_out):
    experts = lax.axis_size("expert")
    tok_dev, top_count = expert_ids.shape
    d_model = tokens.shape[1]
    assert sum(CHUNKS) == MOST
    expert_range = jnp.arange(experts, dtype=jnp.int32)
    placed = (host[:, None] == expert_range[None, :]).astype(jnp.int32)
    holder = jnp.sum(placed * expert_range[:, None], axis=0)
    flat_experts = expert_ids.reshape(-1)
    onehot = (flat_experts[:, None] == expert_range[None, :]).astype(jnp.int32)
    within = jnp.sum(jnp.cumsum(onehot, axis=0) * onehot, axis=1) - 1
    target = jnp.sum(onehot * holder[None, :], axis=1)
    piece = d_model // PIECES
    within_rep = jnp.repeat(within.reshape(tok_dev, top_count), PIECES, axis=0)
    target_rep = jnp.repeat(target.reshape(tok_dev, top_count), PIECES, axis=0)
    token_pieces = tokens.reshape(tok_dev * PIECES, piece)
    piece_rows = jnp.arange(tok_dev * PIECES, dtype=jnp.int32)
    gate_rep = jnp.repeat(gate_weights, PIECES, axis=0)
    both = None
    first_slot = 0
    for chunk_slots in CHUNKS:
        chunk_rows = experts * chunk_slots
        piece_cols = jnp.arange(chunk_rows * PIECES, dtype=jnp.int32)
        same_piece = (piece_rows[:, None] % PIECES) == (piece_cols[None, :] % PIECES)
        slot_col = piece_cols[None, :] // PIECES
        inside = (within_rep >= first_slot) & (within_rep < first_slot + chunk_slots)
        slot_id = jnp.where(inside, target_rep * chunk_slots + within_rep - first_slot, -1)
        first_slot += chunk_slots
        taken = jnp.zeros((tok_dev * PIECES, chunk_rows * PIECES), jnp.bool_)
        combine = jnp.zeros((tok_dev * PIECES, chunk_rows * PIECES), jnp.float32)
        for k in range(top_count):
            match = slot_id[:, k : k + 1] == slot_col
            taken = taken | match
            combine = combine + jnp.where(match, gate_rep[:, k : k + 1], jnp.float32(0.0))
        taken = taken & same_piece
        combine = jnp.where(same_piece, combine, jnp.float32(0.0))
        dispatch = taken.T.astype(jnp.bfloat16)
        outgoing = jnp.dot(dispatch, token_pieces, preferred_element_type=jnp.float32).astype(jnp.bfloat16)
        received = lax.all_to_all(
            outgoing.reshape(experts, chunk_slots * PIECES, piece),
            "expert",
            split_axis=0,
            concat_axis=0,
            tiled=True,
        )
        expert_out = expert_ffn(received.reshape(chunk_rows, d_model), w_in[0], w_out[0])
        answered = lax.all_to_all(
            expert_out.reshape(experts, chunk_slots * PIECES, piece),
            "expert",
            split_axis=0,
            concat_axis=0,
            tiled=True,
        ).reshape(chunk_rows * PIECES, piece)
        combine_hi = combine.astype(jnp.bfloat16)
        combine_lo = (combine - combine_hi.astype(jnp.float32)).astype(jnp.bfloat16)
        stacked = jnp.concatenate([combine_hi, combine_lo], axis=0)
        part = jnp.dot(stacked, answered, preferred_element_type=jnp.float32)
        both = part if both is None else both + part
    half = tok_dev * PIECES
    weighted = (both[:half] + both[half:]).reshape(tok_dev, d_model)
    return weighted.astype(jnp.bfloat16)


def solution(mesh):
    in_specs = (
        P("expert", None),
        P("expert", None),
        P("expert", None),
        P(),
        P("expert", None, None, None, None),
        P("expert", None, None, None),
    )
    out_specs = P("expert", None)
    return jax.shard_map(local, mesh=mesh, in_specs=in_specs, out_specs=out_specs, check_vma=False)
```

```python
import jax
import jax.numpy as jnp
from jax import lax
from jax.sharding import PartitionSpec as P

MOST = 6
CHUNKS = ((4, 2), (2, 4))


def expert_ffn(rows, first_weights, second_weights):
    projected = jnp.einsum(
        "rd,hdgu->rhgu", rows, first_weights, preferred_element_type=jnp.float32
    )
    hidden = (jax.nn.silu(projected[:, :, 0]) * projected[:, :, 1]).astype(jnp.bfloat16)
    output = jnp.einsum(
        "rhu,hud->rd", hidden, second_weights, preferred_element_type=jnp.float32
    )
    return output.astype(jnp.bfloat16)


def local(tokens, expert_ids, gate_weights, host, w_in, w_out):
    experts = lax.axis_size("expert")
    tok_dev, top_count = expert_ids.shape
    d_model = tokens.shape[1]
    assert sum(slots for slots, _ in CHUNKS) == MOST
    expert_range = jnp.arange(experts, dtype=jnp.int32)
    placed = (host[:, None] == expert_range[None, :]).astype(jnp.int32)
    holder = jnp.sum(placed * expert_range[:, None], axis=0)
    flat_experts = expert_ids.reshape(-1)
    onehot = (flat_experts[:, None] == expert_range[None, :]).astype(jnp.int32)
    within = jnp.sum(jnp.cumsum(onehot, axis=0) * onehot, axis=1) - 1
    target = jnp.sum(onehot * holder[None, :], axis=1)
    within_of = within.reshape(tok_dev, top_count)
    target_of = target.reshape(tok_dev, top_count)
    weighted = None
    first_slot = 0
    for chunk_slots, pieces in CHUNKS:
        piece = d_model // pieces
        chunk_rows = experts * chunk_slots
        within_rep = jnp.repeat(within_of, pieces, axis=0)
        target_rep = jnp.repeat(target_of, pieces, axis=0)
        gate_rep = jnp.repeat(gate_weights, pieces, axis=0)
        token_pieces = tokens.reshape(tok_dev * pieces, piece)
        piece_rows = jnp.arange(tok_dev * pieces, dtype=jnp.int32)
        piece_cols = jnp.arange(chunk_rows * pieces, dtype=jnp.int32)
        same_piece = (piece_rows[:, None] % pieces) == (piece_cols[None, :] % pieces)
        slot_col = piece_cols[None, :] // pieces
        inside = (within_rep >= first_slot) & (within_rep < first_slot + chunk_slots)
        slot_id = jnp.where(inside, target_rep * chunk_slots + within_rep - first_slot, -1)
        first_slot += chunk_slots
        taken = jnp.zeros((tok_dev * pieces, chunk_rows * pieces), jnp.bool_)
        combine = jnp.zeros((tok_dev * pieces, chunk_rows * pieces), jnp.float32)
        for k in range(top_count):
            match = slot_id[:, k : k + 1] == slot_col
            taken = taken | match
            combine = combine + jnp.where(match, gate_rep[:, k : k + 1], jnp.float32(0.0))
        taken = taken & same_piece
        combine = jnp.where(same_piece, combine, jnp.float32(0.0))
        dispatch = taken.T.astype(jnp.bfloat16)
        outgoing = jnp.dot(dispatch, token_pieces, preferred_element_type=jnp.float32).astype(jnp.bfloat16)
        received = lax.all_to_all(
            outgoing.reshape(experts, chunk_slots * pieces, piece),
            "expert",
            split_axis=0,
            concat_axis=0,
            tiled=True,
        )
        expert_out = expert_ffn(received.reshape(chunk_rows, d_model), w_in[0], w_out[0])
        answered = lax.all_to_all(
            expert_out.reshape(experts, chunk_slots * pieces, piece),
            "expert",
            split_axis=0,
            concat_axis=0,
            tiled=True,
        ).reshape(chunk_rows * pieces, piece)
        combine_hi = combine.astype(jnp.bfloat16)
        combine_lo = (combine - combine_hi.astype(jnp.float32)).astype(jnp.bfloat16)
        stacked = jnp.concatenate([combine_hi, combine_lo], axis=0)
        part = jnp.dot(stacked, answered, preferred_element_type=jnp.float32)
        half = tok_dev * pieces
        part = (part[:half] + part[half:]).reshape(tok_dev, d_model)
        weighted = part if weighted is None else weighted + part
    return weighted.astype(jnp.bfloat16)


def solution(mesh):
    in_specs = (
        P("expert", None),
        P("expert", None),
        P("expert", None),
        P(),
        P("expert", None, None, None, None),
        P("expert", None, None, None),
    )
    out_specs = P("expert", None)
    return jax.shard_map(local, mesh=mesh, in_specs=in_specs, out_specs=out_specs, check_vma=False)
```

```python
import jax
import jax.numpy as jnp
from jax import lax
from jax.sharding import PartitionSpec as P

MOST = 6
CHUNKS = ((4, 2), (2, 4))


def expert_ffn(rows, first_weights, second_weights):
    projected = jnp.einsum(
        "rd,hdgu->rhgu", rows, first_weights, preferred_element_type=jnp.float32
    )
    hidden = (jax.nn.silu(projected[:, :, 0]) * projected[:, :, 1]).astype(jnp.bfloat16)
    hidden = lax.optimization_barrier(hidden)
    output = jnp.einsum(
        "rhu,hud->rd", hidden, second_weights, preferred_element_type=jnp.float32
    )
    return output.astype(jnp.bfloat16)


def local(tokens, expert_ids, gate_weights, host, w_in, w_out):
    experts = lax.axis_size("expert")
    tok_dev, top_count = expert_ids.shape
    d_model = tokens.shape[1]
    assert sum(slots for slots, _ in CHUNKS) == MOST
    expert_range = jnp.arange(experts, dtype=jnp.int32)
    placed = (host[:, None] == expert_range[None, :]).astype(jnp.int32)
    holder = jnp.sum(placed * expert_range[:, None], axis=0)
    flat_experts = expert_ids.reshape(-1)
    onehot = (flat_experts[:, None] == expert_range[None, :]).astype(jnp.int32)
    within = jnp.sum(jnp.cumsum(onehot, axis=0) * onehot, axis=1) - 1
    target = jnp.sum(onehot * holder[None, :], axis=1)
    within_of = within.reshape(tok_dev, top_count)
    target_of = target.reshape(tok_dev, top_count)
    weighted = None
    first_slot = 0
    for chunk_slots, pieces in CHUNKS:
        piece = d_model // pieces
        chunk_rows = experts * chunk_slots
        within_rep = jnp.repeat(within_of, pieces, axis=0)
        target_rep = jnp.repeat(target_of, pieces, axis=0)
        gate_rep = jnp.repeat(gate_weights, pieces, axis=0)
        token_pieces = tokens.reshape(tok_dev * pieces, piece)
        piece_rows = jnp.arange(tok_dev * pieces, dtype=jnp.int32)
        piece_cols = jnp.arange(chunk_rows * pieces, dtype=jnp.int32)
        same_piece = (piece_rows[:, None] % pieces) == (piece_cols[None, :] % pieces)
        slot_col = piece_cols[None, :] // pieces
        inside = (within_rep >= first_slot) & (within_rep < first_slot + chunk_slots)
        slot_id = jnp.where(inside, target_rep * chunk_slots + within_rep - first_slot, -1)
        first_slot += chunk_slots
        taken = jnp.zeros((tok_dev * pieces, chunk_rows * pieces), jnp.bool_)
        combine = jnp.zeros((tok_dev * pieces, chunk_rows * pieces), jnp.float32)
        for k in range(top_count):
            match = slot_id[:, k : k + 1] == slot_col
            taken = taken | match
            combine = combine + jnp.where(match, gate_rep[:, k : k + 1], jnp.float32(0.0))
        taken = taken & same_piece
        combine = jnp.where(same_piece, combine, jnp.float32(0.0))
        dispatch = taken.T.astype(jnp.bfloat16)
        outgoing = jnp.dot(dispatch, token_pieces, preferred_element_type=jnp.float32).astype(jnp.bfloat16)
        received = lax.all_to_all(
            outgoing.reshape(experts, chunk_slots * pieces, piece),
            "expert",
            split_axis=0,
            concat_axis=0,
            tiled=True,
        )
        expert_out = expert_ffn(received.reshape(chunk_rows, d_model), w_in[0], w_out[0])
        answered = lax.all_to_all(
            expert_out.reshape(experts, chunk_slots * pieces, piece),
            "expert",
            split_axis=0,
            concat_axis=0,
            tiled=True,
        ).reshape(chunk_rows * pieces, piece)
        combine_hi = combine.astype(jnp.bfloat16)
        combine_lo = (combine - combine_hi.astype(jnp.float32)).astype(jnp.bfloat16)
        stacked = jnp.concatenate([combine_hi, combine_lo], axis=0)
        part = jnp.dot(stacked, answered, preferred_element_type=jnp.float32)
        half = tok_dev * pieces
        part = (part[:half] + part[half:]).reshape(tok_dev, d_model)
        weighted = part if weighted is None else weighted + part
    return weighted.astype(jnp.bfloat16)


def solution(mesh):
    in_specs = (
        P("expert", None),
        P("expert", None),
        P("expert", None),
        P(),
        P("expert", None, None, None, None),
        P("expert", None, None, None),
    )
    out_specs = P("expert", None)
    return jax.shard_map(local, mesh=mesh, in_specs=in_specs, out_specs=out_specs, check_vma=False)
```

```python
import jax
import jax.numpy as jnp
from jax import lax
from jax.sharding import PartitionSpec as P

MOST = 6
CHUNKS = ((4, 2), (2, 4))


def expert_ffn(rows, first_weights, second_weights):
    projected = jnp.einsum(
        "rd,hdgu->rhgu", rows, first_weights, preferred_element_type=jnp.float32
    )
    hidden = (jax.nn.silu(projected[:, :, 0]) * projected[:, :, 1]).astype(jnp.bfloat16)
    units = hidden.shape[1] * hidden.shape[2]
    output = jnp.dot(
        hidden.reshape(hidden.shape[0], units),
        second_weights.reshape(units, second_weights.shape[2]),
        preferred_element_type=jnp.float32,
    )
    return output.astype(jnp.bfloat16)


def local(tokens, expert_ids, gate_weights, host, w_in, w_out):
    experts = lax.axis_size("expert")
    tok_dev, top_count = expert_ids.shape
    d_model = tokens.shape[1]
    assert sum(slots for slots, _ in CHUNKS) == MOST
    expert_range = jnp.arange(experts, dtype=jnp.int32)
    placed = (host[:, None] == expert_range[None, :]).astype(jnp.int32)
    holder = jnp.sum(placed * expert_range[:, None], axis=0)
    flat_experts = expert_ids.reshape(-1)
    onehot = (flat_experts[:, None] == expert_range[None, :]).astype(jnp.int32)
    within = jnp.sum(jnp.cumsum(onehot, axis=0) * onehot, axis=1) - 1
    target = jnp.sum(onehot * holder[None, :], axis=1)
    within_of = within.reshape(tok_dev, top_count)
    target_of = target.reshape(tok_dev, top_count)
    weighted = None
    first_slot = 0
    for chunk_slots, pieces in CHUNKS:
        piece = d_model // pieces
        chunk_rows = experts * chunk_slots
        within_rep = jnp.repeat(within_of, pieces, axis=0)
        target_rep = jnp.repeat(target_of, pieces, axis=0)
        gate_rep = jnp.repeat(gate_weights, pieces, axis=0)
        token_pieces = tokens.reshape(tok_dev * pieces, piece)
        piece_rows = jnp.arange(tok_dev * pieces, dtype=jnp.int32)
        piece_cols = jnp.arange(chunk_rows * pieces, dtype=jnp.int32)
        same_piece = (piece_rows[:, None] % pieces) == (piece_cols[None, :] % pieces)
        slot_col = piece_cols[None, :] // pieces
        inside = (within_rep >= first_slot) & (within_rep < first_slot + chunk_slots)
        slot_id = jnp.where(inside, target_rep * chunk_slots + within_rep - first_slot, -1)
        first_slot += chunk_slots
        taken = jnp.zeros((tok_dev * pieces, chunk_rows * pieces), jnp.bool_)
        combine = jnp.zeros((tok_dev * pieces, chunk_rows * pieces), jnp.float32)
        for k in range(top_count):
            match = slot_id[:, k : k + 1] == slot_col
            taken = taken | match
            combine = combine + jnp.where(match, gate_rep[:, k : k + 1], jnp.float32(0.0))
        taken = taken & same_piece
        combine = jnp.where(same_piece, combine, jnp.float32(0.0))
        dispatch = taken.T.astype(jnp.bfloat16)
        outgoing = jnp.dot(dispatch, token_pieces, preferred_element_type=jnp.float32).astype(jnp.bfloat16)
        received = lax.all_to_all(
            outgoing.reshape(experts, chunk_slots * pieces, piece),
            "expert",
            split_axis=0,
            concat_axis=0,
            tiled=True,
        )
        expert_out = expert_ffn(received.reshape(chunk_rows, d_model), w_in[0], w_out[0])
        answered = lax.all_to_all(
            expert_out.reshape(experts, chunk_slots * pieces, piece),
            "expert",
            split_axis=0,
            concat_axis=0,
            tiled=True,
        ).reshape(chunk_rows * pieces, piece)
        combine_hi = combine.astype(jnp.bfloat16)
        combine_lo = (combine - combine_hi.astype(jnp.float32)).astype(jnp.bfloat16)
        stacked = jnp.concatenate([combine_hi, combine_lo], axis=0)
        part = jnp.dot(stacked, answered, preferred_element_type=jnp.float32)
        half = tok_dev * pieces
        part = (part[:half] + part[half:]).reshape(tok_dev, d_model)
        weighted = part if weighted is None else weighted + part
    return weighted.astype(jnp.bfloat16)


def solution(mesh):
    in_specs = (
        P("expert", None),
        P("expert", None),
        P("expert", None),
        P(),
        P("expert", None, None, None, None),
        P("expert", None, None, None),
    )
    out_specs = P("expert", None)
    return jax.shard_map(local, mesh=mesh, in_specs=in_specs, out_specs=out_specs, check_vma=False)
```

```python
import jax
import jax.numpy as jnp
from jax import lax
from jax.sharding import PartitionSpec as P

MOST = 6
CHUNKS = ((4, 2), (2, 4))


def expert_ffn(rows, first_weights, second_weights):
    projected = jnp.einsum(
        "rd,hdgu->rhgu", rows, first_weights, preferred_element_type=jnp.float32
    )
    hidden = (jax.nn.silu(projected[:, :, 0]) * projected[:, :, 1]).astype(jnp.bfloat16)
    output = jnp.dot(hidden[:, 0], second_weights[0], preferred_element_type=jnp.float32)
    for half in range(1, hidden.shape[1]):
        output = output + jnp.dot(
            hidden[:, half], second_weights[half], preferred_element_type=jnp.float32
        )
    return output.astype(jnp.bfloat16)


def local(tokens, expert_ids, gate_weights, host, w_in, w_out):
    experts = lax.axis_size("expert")
    tok_dev, top_count = expert_ids.shape
    d_model = tokens.shape[1]
    assert sum(slots for slots, _ in CHUNKS) == MOST
    expert_range = jnp.arange(experts, dtype=jnp.int32)
    placed = (host[:, None] == expert_range[None, :]).astype(jnp.int32)
    holder = jnp.sum(placed * expert_range[:, None], axis=0)
    flat_experts = expert_ids.reshape(-1)
    onehot = (flat_experts[:, None] == expert_range[None, :]).astype(jnp.int32)
    within = jnp.sum(jnp.cumsum(onehot, axis=0) * onehot, axis=1) - 1
    target = jnp.sum(onehot * holder[None, :], axis=1)
    within_of = within.reshape(tok_dev, top_count)
    target_of = target.reshape(tok_dev, top_count)
    weighted = None
    first_slot = 0
    for chunk_slots, pieces in CHUNKS:
        piece = d_model // pieces
        chunk_rows = experts * chunk_slots
        within_rep = jnp.repeat(within_of, pieces, axis=0)
        target_rep = jnp.repeat(target_of, pieces, axis=0)
        gate_rep = jnp.repeat(gate_weights, pieces, axis=0)
        token_pieces = tokens.reshape(tok_dev * pieces, piece)
        piece_rows = jnp.arange(tok_dev * pieces, dtype=jnp.int32)
        piece_cols = jnp.arange(chunk_rows * pieces, dtype=jnp.int32)
        same_piece = (piece_rows[:, None] % pieces) == (piece_cols[None, :] % pieces)
        slot_col = piece_cols[None, :] // pieces
        inside = (within_rep >= first_slot) & (within_rep < first_slot + chunk_slots)
        slot_id = jnp.where(inside, target_rep * chunk_slots + within_rep - first_slot, -1)
        first_slot += chunk_slots
        taken = jnp.zeros((tok_dev * pieces, chunk_rows * pieces), jnp.bool_)
        combine = jnp.zeros((tok_dev * pieces, chunk_rows * pieces), jnp.float32)
        for k in range(top_count):
            match = slot_id[:, k : k + 1] == slot_col
            taken = taken | match
            combine = combine + jnp.where(match, gate_rep[:, k : k + 1], jnp.float32(0.0))
        taken = taken & same_piece
        combine = jnp.where(same_piece, combine, jnp.float32(0.0))
        dispatch = taken.T.astype(jnp.bfloat16)
        outgoing = jnp.dot(dispatch, token_pieces, preferred_element_type=jnp.float32).astype(jnp.bfloat16)
        received = lax.all_to_all(
            outgoing.reshape(experts, chunk_slots * pieces, piece),
            "expert",
            split_axis=0,
            concat_axis=0,
            tiled=True,
        )
        expert_out = expert_ffn(received.reshape(chunk_rows, d_model), w_in[0], w_out[0])
        answered = lax.all_to_all(
            expert_out.reshape(experts, chunk_slots * pieces, piece),
            "expert",
            split_axis=0,
            concat_axis=0,
            tiled=True,
        ).reshape(chunk_rows * pieces, piece)
        combine_hi = combine.astype(jnp.bfloat16)
        combine_lo = (combine - combine_hi.astype(jnp.float32)).astype(jnp.bfloat16)
        stacked = jnp.concatenate([combine_hi, combine_lo], axis=0)
        part = jnp.dot(stacked, answered, preferred_element_type=jnp.float32)
        half = tok_dev * pieces
        part = (part[:half] + part[half:]).reshape(tok_dev, d_model)
        weighted = part if weighted is None else weighted + part
    return weighted.astype(jnp.bfloat16)


def solution(mesh):
    in_specs = (
        P("expert", None),
        P("expert", None),
        P("expert", None),
        P(),
        P("expert", None, None, None, None),
        P("expert", None, None, None),
    )
    out_specs = P("expert", None)
    return jax.shard_map(local, mesh=mesh, in_specs=in_specs, out_specs=out_specs, check_vma=False)
```

```python
import jax
import jax.numpy as jnp
from jax import lax
from jax.sharding import PartitionSpec as P

MOST = 6
CHUNKS = ((4, 2), (2, 4))


def expert_ffn(rows, first_weights, second_weights, split_halves):
    projected = jnp.einsum(
        "rd,hdgu->rhgu", rows, first_weights, preferred_element_type=jnp.float32
    )
    hidden = (jax.nn.silu(projected[:, :, 0]) * projected[:, :, 1]).astype(jnp.bfloat16)
    if not split_halves:
        output = jnp.einsum(
            "rhu,hud->rd", hidden, second_weights, preferred_element_type=jnp.float32
        )
        return output.astype(jnp.bfloat16)
    output = jnp.dot(hidden[:, 0], second_weights[0], preferred_element_type=jnp.float32)
    for half in range(1, hidden.shape[1]):
        output = output + jnp.dot(
            hidden[:, half], second_weights[half], preferred_element_type=jnp.float32
        )
    return output.astype(jnp.bfloat16)


def local(tokens, expert_ids, gate_weights, host, w_in, w_out):
    experts = lax.axis_size("expert")
    tok_dev, top_count = expert_ids.shape
    d_model = tokens.shape[1]
    assert sum(slots for slots, _ in CHUNKS) == MOST
    expert_range = jnp.arange(experts, dtype=jnp.int32)
    placed = (host[:, None] == expert_range[None, :]).astype(jnp.int32)
    holder = jnp.sum(placed * expert_range[:, None], axis=0)
    flat_experts = expert_ids.reshape(-1)
    onehot = (flat_experts[:, None] == expert_range[None, :]).astype(jnp.int32)
    within = jnp.sum(jnp.cumsum(onehot, axis=0) * onehot, axis=1) - 1
    target = jnp.sum(onehot * holder[None, :], axis=1)
    within_of = within.reshape(tok_dev, top_count)
    target_of = target.reshape(tok_dev, top_count)
    weighted = None
    first_slot = 0
    for chunk_slots, pieces in CHUNKS:
        piece = d_model // pieces
        chunk_rows = experts * chunk_slots
        within_rep = jnp.repeat(within_of, pieces, axis=0)
        target_rep = jnp.repeat(target_of, pieces, axis=0)
        gate_rep = jnp.repeat(gate_weights, pieces, axis=0)
        token_pieces = tokens.reshape(tok_dev * pieces, piece)
        piece_rows = jnp.arange(tok_dev * pieces, dtype=jnp.int32)
        piece_cols = jnp.arange(chunk_rows * pieces, dtype=jnp.int32)
        same_piece = (piece_rows[:, None] % pieces) == (piece_cols[None, :] % pieces)
        slot_col = piece_cols[None, :] // pieces
        inside = (within_rep >= first_slot) & (within_rep < first_slot + chunk_slots)
        slot_id = jnp.where(inside, target_rep * chunk_slots + within_rep - first_slot, -1)
        first_slot += chunk_slots
        taken = jnp.zeros((tok_dev * pieces, chunk_rows * pieces), jnp.bool_)
        combine = jnp.zeros((tok_dev * pieces, chunk_rows * pieces), jnp.float32)
        for k in range(top_count):
            match = slot_id[:, k : k + 1] == slot_col
            taken = taken | match
            combine = combine + jnp.where(match, gate_rep[:, k : k + 1], jnp.float32(0.0))
        taken = taken & same_piece
        combine = jnp.where(same_piece, combine, jnp.float32(0.0))
        dispatch = taken.T.astype(jnp.bfloat16)
        outgoing = jnp.dot(dispatch, token_pieces, preferred_element_type=jnp.float32).astype(jnp.bfloat16)
        received = lax.all_to_all(
            outgoing.reshape(experts, chunk_slots * pieces, piece),
            "expert",
            split_axis=0,
            concat_axis=0,
            tiled=True,
        )
        expert_out = expert_ffn(
            received.reshape(chunk_rows, d_model), w_in[0], w_out[0], chunk_slots > 2
        )
        answered = lax.all_to_all(
            expert_out.reshape(experts, chunk_slots * pieces, piece),
            "expert",
            split_axis=0,
            concat_axis=0,
            tiled=True,
        ).reshape(chunk_rows * pieces, piece)
        combine_hi = combine.astype(jnp.bfloat16)
        combine_lo = (combine - combine_hi.astype(jnp.float32)).astype(jnp.bfloat16)
        stacked = jnp.concatenate([combine_hi, combine_lo], axis=0)
        part = jnp.dot(stacked, answered, preferred_element_type=jnp.float32)
        half = tok_dev * pieces
        part = (part[:half] + part[half:]).reshape(tok_dev, d_model)
        weighted = part if weighted is None else weighted + part
    return weighted.astype(jnp.bfloat16)


def solution(mesh):
    in_specs = (
        P("expert", None),
        P("expert", None),
        P("expert", None),
        P(),
        P("expert", None, None, None, None),
        P("expert", None, None, None),
    )
    out_specs = P("expert", None)
    return jax.shard_map(local, mesh=mesh, in_specs=in_specs, out_specs=out_specs, check_vma=False)
```

```python
import jax
import jax.numpy as jnp
from jax import lax
from jax.sharding import PartitionSpec as P

MOST = 6
CHUNKS = ((4, 2), (2, 4))


def expert_ffn(rows, first_weights, second_weights):
    projected = jnp.einsum(
        "rd,hdgu->rhgu", rows, first_weights, preferred_element_type=jnp.float32
    )
    hidden = (jax.nn.silu(projected[:, :, 0]) * projected[:, :, 1]).astype(jnp.bfloat16)
    output = jnp.einsum(
        "rhu,hud->rd", hidden, second_weights, preferred_element_type=jnp.float32
    )
    return output.astype(jnp.bfloat16)


def local(tokens, expert_ids, gate_weights, host, w_in, w_out):
    experts = lax.axis_size("expert")
    tok_dev, top_count = expert_ids.shape
    d_model = tokens.shape[1]
    assert sum(slots for slots, _ in CHUNKS) == MOST
    expert_range = jnp.arange(experts, dtype=jnp.int32)
    placed = (host[:, None] == expert_range[None, :]).astype(jnp.int32)
    holder = jnp.sum(placed * expert_range[:, None], axis=0)
    flat_experts = expert_ids.reshape(-1)
    onehot = (flat_experts[:, None] == expert_range[None, :]).astype(jnp.int32)
    within = jnp.sum(jnp.cumsum(onehot, axis=0) * onehot, axis=1) - 1
    target = jnp.sum(onehot * holder[None, :], axis=1)
    within_of = within.reshape(tok_dev, top_count)
    target_of = target.reshape(tok_dev, top_count)
    weighted = None
    first_slot = 0
    for chunk_slots, pieces in CHUNKS:
        piece = d_model // pieces
        chunk_rows = experts * chunk_slots
        within_rep = jnp.repeat(within_of, pieces, axis=0)
        target_rep = jnp.repeat(target_of, pieces, axis=0)
        gate_rep = jnp.repeat(gate_weights, pieces, axis=0)
        token_pieces = tokens.reshape(tok_dev * pieces, piece)
        piece_rows = jnp.arange(tok_dev * pieces, dtype=jnp.int32)
        piece_cols = jnp.arange(chunk_rows * pieces, dtype=jnp.int32)
        same_piece = (piece_rows[:, None] % pieces) == (piece_cols[None, :] % pieces)
        slot_col = piece_cols[None, :] // pieces
        inside = (within_rep >= first_slot) & (within_rep < first_slot + chunk_slots)
        slot_id = jnp.where(inside, target_rep * chunk_slots + within_rep - first_slot, -1)
        first_slot += chunk_slots
        taken = jnp.zeros((tok_dev * pieces, chunk_rows * pieces), jnp.bool_)
        combine = jnp.zeros((tok_dev * pieces, chunk_rows * pieces), jnp.float32)
        for k in range(top_count):
            match = slot_id[:, k : k + 1] == slot_col
            taken = taken | match
            combine = combine + jnp.where(match, gate_rep[:, k : k + 1], jnp.float32(0.0))
        taken = taken & same_piece
        combine = jnp.where(same_piece, combine, jnp.float32(0.0))
        dispatch = taken.T.astype(jnp.bfloat16)
        outgoing = jnp.dot(dispatch, token_pieces, preferred_element_type=jnp.float32).astype(jnp.bfloat16)
        received = lax.all_to_all(
            outgoing.reshape(experts, chunk_slots * pieces, piece),
            "expert",
            split_axis=0,
            concat_axis=0,
            tiled=True,
        )
        expert_out = expert_ffn(received.reshape(chunk_rows, d_model), w_in[0], w_out[0])
        answered = lax.all_to_all(
            expert_out.reshape(experts, chunk_slots * pieces, piece),
            "expert",
            split_axis=0,
            concat_axis=0,
            tiled=True,
        ).reshape(chunk_rows * pieces, piece)
        part = jnp.dot(
            combine.astype(jnp.bfloat16), answered, preferred_element_type=jnp.float32
        ).reshape(tok_dev, d_model)
        weighted = part if weighted is None else weighted + part
    return weighted.astype(jnp.bfloat16)


def solution(mesh):
    in_specs = (
        P("expert", None),
        P("expert", None),
        P("expert", None),
        P(),
        P("expert", None, None, None, None),
        P("expert", None, None, None),
    )
    out_specs = P("expert", None)
    return jax.shard_map(local, mesh=mesh, in_specs=in_specs, out_specs=out_specs, check_vma=False)
```

```python
import jax
import jax.numpy as jnp
from jax import lax
from jax.sharding import PartitionSpec as P

MOST = 6
CHUNKS = ((4, 2), (2, 4))


def expert_ffn(rows, first_weights, second_weights, split_halves):
    projected = jnp.einsum(
        "rd,hdgu->rhgu", rows, first_weights, preferred_element_type=jnp.float32
    )
    hidden = (jax.nn.silu(projected[:, :, 0]) * projected[:, :, 1]).astype(jnp.bfloat16)
    if not split_halves:
        output = jnp.einsum(
            "rhu,hud->rd", hidden, second_weights, preferred_element_type=jnp.float32
        )
        return output.astype(jnp.bfloat16)
    output = jnp.dot(hidden[:, 0], second_weights[0], preferred_element_type=jnp.float32)
    for half in range(1, hidden.shape[1]):
        output = output + jnp.dot(
            hidden[:, half], second_weights[half], preferred_element_type=jnp.float32
        )
    return output.astype(jnp.bfloat16)


def local(tokens, expert_ids, gate_weights, host, w_in, w_out):
    experts = lax.axis_size("expert")
    tok_dev, top_count = expert_ids.shape
    d_model = tokens.shape[1]
    assert sum(slots for slots, _ in CHUNKS) == MOST
    expert_range = jnp.arange(experts, dtype=jnp.int32)
    placed = (host[:, None] == expert_range[None, :]).astype(jnp.int32)
    holder = jnp.sum(placed * expert_range[:, None], axis=0)
    flat_experts = expert_ids.reshape(-1)
    onehot = (flat_experts[:, None] == expert_range[None, :]).astype(jnp.int32)
    within = jnp.sum(jnp.cumsum(onehot, axis=0) * onehot, axis=1) - 1
    target = jnp.sum(onehot * holder[None, :], axis=1)
    within_of = within.reshape(tok_dev, top_count)
    target_of = target.reshape(tok_dev, top_count)
    weighted = None
    first_slot = 0
    for chunk_slots, pieces in CHUNKS:
        piece = d_model // pieces
        chunk_rows = experts * chunk_slots
        within_rep = jnp.repeat(within_of, pieces, axis=0)
        target_rep = jnp.repeat(target_of, pieces, axis=0)
        gate_rep = jnp.repeat(gate_weights, pieces, axis=0)
        token_pieces = tokens.reshape(tok_dev * pieces, piece)
        piece_rows = jnp.arange(tok_dev * pieces, dtype=jnp.int32)
        piece_cols = jnp.arange(chunk_rows * pieces, dtype=jnp.int32)
        same_piece = (piece_rows[:, None] % pieces) == (piece_cols[None, :] % pieces)
        slot_col = piece_cols[None, :] // pieces
        inside = (within_rep >= first_slot) & (within_rep < first_slot + chunk_slots)
        slot_id = jnp.where(inside, target_rep * chunk_slots + within_rep - first_slot, -1)
        first_slot += chunk_slots
        taken = jnp.zeros((tok_dev * pieces, chunk_rows * pieces), jnp.bool_)
        combine = jnp.zeros((tok_dev * pieces, chunk_rows * pieces), jnp.float32)
        for k in range(top_count):
            match = slot_id[:, k : k + 1] == slot_col
            taken = taken | match
            combine = combine + jnp.where(match, gate_rep[:, k : k + 1], jnp.float32(0.0))
        taken = taken & same_piece
        combine = jnp.where(same_piece, combine, jnp.float32(0.0))
        dispatch = taken.T.astype(jnp.bfloat16)
        outgoing = jnp.dot(dispatch, token_pieces, preferred_element_type=jnp.float32).astype(jnp.bfloat16)
        received = lax.all_to_all(
            outgoing.reshape(experts, chunk_slots * pieces, piece),
            "expert",
            split_axis=0,
            concat_axis=0,
            tiled=True,
        )
        expert_out = expert_ffn(
            received.reshape(chunk_rows, d_model), w_in[0], w_out[0], chunk_slots > 2
        )
        answered = lax.all_to_all(
            expert_out.reshape(experts, chunk_slots * pieces, piece),
            "expert",
            split_axis=0,
            concat_axis=0,
            tiled=True,
        ).reshape(chunk_rows * pieces, piece)
        part = jnp.dot(
            combine.astype(jnp.bfloat16), answered, preferred_element_type=jnp.float32
        ).reshape(tok_dev, d_model)
        weighted = part if weighted is None else weighted + part
    return weighted.astype(jnp.bfloat16)


def solution(mesh):
    in_specs = (
        P("expert", None),
        P("expert", None),
        P("expert", None),
        P(),
        P("expert", None, None, None, None),
        P("expert", None, None, None),
    )
    out_specs = P("expert", None)
    return jax.shard_map(local, mesh=mesh, in_specs=in_specs, out_specs=out_specs, check_vma=False)
```

```python
import jax
import jax.numpy as jnp
from jax import lax
from jax.sharding import PartitionSpec as P

MOST = 6
CHUNKS = ((4, 2), (2, 4))


def expert_ffn(rows, first_weights, second_weights):
    projected = jnp.einsum(
        "rd,hdgu->rhgu", rows, first_weights, preferred_element_type=jnp.float32
    )
    hidden = (jax.nn.silu(projected[:, :, 0]) * projected[:, :, 1]).astype(jnp.bfloat16)
    output = jnp.einsum(
        "rhu,hud->rd", hidden, second_weights, preferred_element_type=jnp.float32
    )
    return output.astype(jnp.bfloat16)


def local(tokens, expert_ids, gate_weights, host, w_in, w_out):
    experts = lax.axis_size("expert")
    tok_dev, top_count = expert_ids.shape
    d_model = tokens.shape[1]
    assert sum(slots for slots, _ in CHUNKS) == MOST
    expert_range = jnp.arange(experts, dtype=jnp.int32)
    placed = (host[:, None] == expert_range[None, :]).astype(jnp.int32)
    holder = jnp.sum(placed * expert_range[:, None], axis=0)
    flat_experts = expert_ids.reshape(-1)
    onehot = (flat_experts[:, None] == expert_range[None, :]).astype(jnp.int32)
    order = jnp.arange(flat_experts.shape[0], dtype=jnp.int32)
    earlier = (flat_experts[None, :] == flat_experts[:, None]) & (order[None, :] < order[:, None])
    within = jnp.sum(earlier.astype(jnp.int32), axis=1)
    target = jnp.sum(onehot * holder[None, :], axis=1)
    within_of = within.reshape(tok_dev, top_count)
    target_of = target.reshape(tok_dev, top_count)
    weighted = None
    first_slot = 0
    for chunk_slots, pieces in CHUNKS:
        piece = d_model // pieces
        chunk_rows = experts * chunk_slots
        within_rep = jnp.repeat(within_of, pieces, axis=0)
        target_rep = jnp.repeat(target_of, pieces, axis=0)
        gate_rep = jnp.repeat(gate_weights, pieces, axis=0)
        token_pieces = tokens.reshape(tok_dev * pieces, piece)
        piece_rows = jnp.arange(tok_dev * pieces, dtype=jnp.int32)
        piece_cols = jnp.arange(chunk_rows * pieces, dtype=jnp.int32)
        same_piece = (piece_rows[:, None] % pieces) == (piece_cols[None, :] % pieces)
        slot_col = piece_cols[None, :] // pieces
        inside = (within_rep >= first_slot) & (within_rep < first_slot + chunk_slots)
        slot_id = jnp.where(inside, target_rep * chunk_slots + within_rep - first_slot, -1)
        first_slot += chunk_slots
        taken = jnp.zeros((tok_dev * pieces, chunk_rows * pieces), jnp.bool_)
        combine = jnp.zeros((tok_dev * pieces, chunk_rows * pieces), jnp.float32)
        for k in range(top_count):
            match = slot_id[:, k : k + 1] == slot_col
            taken = taken | match
            combine = combine + jnp.where(match, gate_rep[:, k : k + 1], jnp.float32(0.0))
        taken = taken & same_piece
        combine = jnp.where(same_piece, combine, jnp.float32(0.0))
        dispatch = taken.T.astype(jnp.bfloat16)
        outgoing = jnp.dot(dispatch, token_pieces, preferred_element_type=jnp.float32).astype(jnp.bfloat16)
        received = lax.all_to_all(
            outgoing.reshape(experts, chunk_slots * pieces, piece),
            "expert",
            split_axis=0,
            concat_axis=0,
            tiled=True,
        )
        expert_out = expert_ffn(received.reshape(chunk_rows, d_model), w_in[0], w_out[0])
        answered = lax.all_to_all(
            expert_out.reshape(experts, chunk_slots * pieces, piece),
            "expert",
            split_axis=0,
            concat_axis=0,
            tiled=True,
        ).reshape(chunk_rows * pieces, piece)
        combine_hi = combine.astype(jnp.bfloat16)
        combine_lo = (combine - combine_hi.astype(jnp.float32)).astype(jnp.bfloat16)
        stacked = jnp.concatenate([combine_hi, combine_lo], axis=0)
        part = jnp.dot(stacked, answered, preferred_element_type=jnp.float32)
        half = tok_dev * pieces
        part = (part[:half] + part[half:]).reshape(tok_dev, d_model)
        weighted = part if weighted is None else weighted + part
    return weighted.astype(jnp.bfloat16)


def solution(mesh):
    in_specs = (
        P("expert", None),
        P("expert", None),
        P("expert", None),
        P(),
        P("expert", None, None, None, None),
        P("expert", None, None, None),
    )
    out_specs = P("expert", None)
    return jax.shard_map(local, mesh=mesh, in_specs=in_specs, out_specs=out_specs, check_vma=False)
```
